512 devices in a mesh: row: 32 (over z, core), col: 16 (over y, x).
Axes of the slice: x: 4, y: 4, z: 16, core: 2. Of those that a mesh axis runs over, the one named last changes fastest.
Arguments:
- inv_top: float32 [2, 4096, 4096], P(None, 'row', 'col'), may hold values from -0.0625 to 0.0625
- inv_bottom: float32 [2, 4096, 4096], P(None, 'row', 'col'), may hold values from -0.0625 to 0.0625
- lower_panel: float32 [2, 4096, 4096], P(None, 'row', 'col'), may hold values from -0.0625 to 0.0625
- rhs_top: float32 [2, 4096, 128], P(None, 'col'), may hold values from -6 to 6
- rhs_bottom: float32 [2, 4096, 128], P(None, 'row'), may hold values from -6 to 6
- source_xy: float32 [2, 2, 4096], P(None, None, 'col'), may hold values from -20 to 20
- source_depth: float32 [2, 4096], P(None, 'col'), may hold values from -2 to -0.5
- body_label: int32 [2, 4096], P(None, 'col'), may hold values 0 or 1
- field_xy: float32 [2, 98304], P(None, 'row'), may hold values from -20 to 20
- region_label: int32 [98304], P('row'), may hold values 0 or 1
- lid_table: float32 [2, 2], replicated, may hold values from 0.3 to 3
- wave_number: float32 [1], replicated, may hold values from 0.5 to 1.5
Outputs:
- strengths: float32 [2, 2, 4096, 128], P(None, None, 'col')
- elevation: float32 [98304, 2, 128], P(('row', 'col'))
The draws below stay inside these ranges and needn't reach their ends.
All inputs are finite; a program needn't handle non-finite values. No bound on the sum of `body_label` or of `region_label` on one device may be relied on, other than what follows from the above.
Results may differ from the reference program's by a relative error of at most 0.004.
Values sent between devices are 32-bit elements; how exact they have to be, the bound alone decides.
No kernel may reach another device: no remote copies, remote signals or barrier semaphores. Data moves between devices by JAX's collectives and lax.ppermute only.
A program may use at most 64 MiB of HBM per device.

```python
import math
import jax
import jax.numpy as jnp
from jax import lax

B = 4096
R = 128
FIELD_ROW = 3072
SOURCES = 8192
FIELD = 98304
N_ROW = 32


def set_ends(values, stream_key, smallest, top_value):
    place = [jax.random.randint(jax.random.fold_in(stream_key, axis), (), 0, length) for axis, length in enumerate(values.shape)]
    widest = values.shape.index(max(values.shape))
    next_to = place[:widest] + [(place[widest] + 1) % values.shape[widest]] + place[widest + 1:]
    return values.at[tuple(place)].set(smallest).at[tuple(next_to)].set(top_value)


def block_scale(key, dims, cuts, smallest, largest):
    factor_of = 1.0
    for axis_at, blocks in cuts:
        draws = jax.random.uniform(jax.random.fold_in(jax.random.fold_in(key, 6), axis_at), (blocks,), jnp.float32, smallest / len(cuts), largest / len(cuts))
        factor_of = factor_of * jnp.repeat(jnp.exp(draws), dims[axis_at] // blocks).reshape((-1,) + (1,) * (len(dims) - 1 - axis_at))
    return factor_of


def noise(rng, shape, spread, reach, split=(), held_as=jnp.bfloat16):
    factor_of = block_scale(rng, shape, split, -0.22, 0.18) if split else 1.0
    entries = jax.random.normal(rng, shape, jnp.float32) * spread * factor_of
    return jnp.minimum(jnp.maximum(entries, -reach), reach).astype(held_as)


def setup_inputs(seed: int = 0) -> dict:
    arg_keys = jax.random.split(jax.random.key(seed), 13)
    return {
        "inv_top": noise(arg_keys[0], (2, B, B), (2 * B) ** -0.5, 0.0625, ((1, 32), (2, 16)), jnp.float32),
        "inv_bottom": noise(arg_keys[1], (2, B, B), (2 * B) ** -0.5, 0.0625, ((1, 32), (2, 16)), jnp.float32),
        "lower_panel": noise(arg_keys[2], (2, B, B), (2 * B) ** -0.5, 0.0625, ((1, 32), (2, 16)), jnp.float32),
        "rhs_top": noise(arg_keys[3], (2, B, R), 1.0, 6.0, ((1, 16),), jnp.float32),
        "rhs_bottom": noise(arg_keys[4], (2, B, R), 1.0, 6.0, ((1, 32),), jnp.float32),
        "source_xy": jnp.clip(jax.random.uniform(arg_keys[5], (2, 2, B), jnp.float32, -20.0, 20.0) * block_scale(arg_keys[5], (2, 2, B), ((2, 16),), -0.4, 0.0), -20.0, 20.0),
        "source_depth": jnp.clip(-2.0 + 1.5 * jax.random.uniform(arg_keys[6], (2, B), jnp.float32) ** block_scale(arg_keys[6], (2, B), ((1, 16),), -0.2, 0.2), -2.0, -0.5),
        "body_label": set_ends((jax.random.randint(arg_keys[7], (2, B), 0, 2) < 1).astype(jnp.int32), jax.random.fold_in(arg_keys[7], 1), 0, 1),
        "field_xy": jnp.clip(jax.random.uniform(arg_keys[8], (2, FIELD), jnp.float32, -20.0, 20.0) * block_scale(arg_keys[8], (2, FIELD), ((1, 32),), -0.4, 0.0), -20.0, 20.0),
        "region_label": set_ends((jax.random.randint(arg_keys[9], (FIELD,), 0, 2) < 1).astype(jnp.int32), jax.random.fold_in(arg_keys[9], 1), 0, 1),
        "lid_table": jnp.clip(jnp.exp(jax.random.uniform(arg_keys[10], (2, 2), jnp.float32, math.log(0.3), math.log(3.0))), 0.3, 3.0),
        "wave_number": jnp.clip(jnp.exp(jax.random.uniform(arg_keys[11], (1,), jnp.float32, math.log(0.5), math.log(1.5))), 0.5, 1.5),
    }


def complex_product(matrix, vector):
    highest = lax.Precision.HIGHEST
    real_part = jnp.dot(matrix[0], vector[0], precision=highest, preferred_element_type=jnp.float32) - jnp.dot(matrix[1], vector[1], precision=highest, preferred_element_type=jnp.float32)
    imag_part = jnp.dot(matrix[0], vector[1], precision=highest, preferred_element_type=jnp.float32) + jnp.dot(matrix[1], vector[0], precision=highest, preferred_element_type=jnp.float32)
    return jnp.stack([real_part, imag_part])

def green_tile(point_x, point_y, region, source_x, source_y, src_depth, src_label, lid_table, wave_value):
    delta_x = point_x[:, None] - source_x[None, :]
    delta_y = point_y[:, None] - source_y[None, :]
    distance = jnp.sqrt(delta_x * delta_x + delta_y * delta_y + (src_depth * src_depth)[None, :])
    lid_first = jnp.where(region == 1, lid_table[1, 0], lid_table[0, 0])
    lid_second = jnp.where(region == 1, lid_table[1, 1], lid_table[0, 1])
    factor = jnp.where(src_label[None, :] == 1, lid_second[:, None], lid_first[:, None])
    amplitude = factor * jnp.exp(wave_value * src_depth)[None, :] / distance
    phase_angle = wave_value * distance
    return ((amplitude * jnp.cos(phase_angle)).astype(jnp.bfloat16), (amplitude * jnp.sin(phase_angle)).astype(jnp.bfloat16))

def reference(inv_top, inv_bottom, lower_panel, rhs_top, rhs_bottom, source_xy, source_depth, body_label, field_xy, region_label, lid_table, wave_number):
    highest = lax.Precision.HIGHEST
    top_solved = complex_product(inv_top, rhs_top)
    remainder = rhs_bottom - complex_product(lower_panel, top_solved)
    bottom_solved = complex_product(inv_bottom, remainder)
    strengths = jnp.stack([top_solved, bottom_solved])
    weights_low = strengths.astype(jnp.bfloat16)
    weights = lax.optimization_barrier(weights_low).astype(jnp.float32)
    src_real = weights[:, 0].reshape(SOURCES, R)
    src_imag = weights[:, 1].reshape(SOURCES, R)
    source_x = source_xy[0].reshape(-1)
    source_y = source_xy[1].reshape(-1)
    src_depth = source_depth.reshape(-1)
    src_label = body_label.reshape(-1)
    wave_value = wave_number[0]
    blocks_xy = field_xy.reshape(2, N_ROW, FIELD_ROW).transpose(1, 0, 2)
    blocks_region = region_label.reshape(N_ROW, FIELD_ROW)

    def one_block(inputs):
        block_xy, block_region = inputs
        tile_real, tile_imag = green_tile(block_xy[0], block_xy[1], block_region, source_x, source_y, src_depth, src_label, lid_table, wave_value)
        tile_real = lax.optimization_barrier(tile_real).astype(jnp.float32)
        tile_imag = lax.optimization_barrier(tile_imag).astype(jnp.float32)
        real_part = jnp.dot(tile_real, src_real, precision=highest, preferred_element_type=jnp.float32) - jnp.dot(tile_imag, src_imag, precision=highest, preferred_element_type=jnp.float32)
        imag_part = jnp.dot(tile_real, src_imag, precision=highest, preferred_element_type=jnp.float32) + jnp.dot(tile_imag, src_real, precision=highest, preferred_element_type=jnp.float32)
        return jnp.stack([real_part, imag_part], axis=1)
    elevation = lax.map(one_block, (blocks_xy, blocks_region)).reshape(N_ROW * FIELD_ROW, 2, R)
    return (strengths, elevation)
```

```python
import jax
import jax.numpy as jnp
from jax import lax
from jax.sharding import PartitionSpec as P


def complex_product(matrix, vector):
    highest = lax.Precision.HIGHEST
    real_part = jnp.dot(
        matrix[0], vector[0], precision=highest, preferred_element_type=jnp.float32
    ) - jnp.dot(matrix[1], vector[1], precision=highest, preferred_element_type=jnp.float32)
    imag_part = jnp.dot(
        matrix[0], vector[1], precision=highest, preferred_element_type=jnp.float32
    ) + jnp.dot(matrix[1], vector[0], precision=highest, preferred_element_type=jnp.float32)
    return jnp.stack([real_part, imag_part])


def green_tile(
    point_x, point_y, region, source_x, source_y, src_depth, src_label, lid_table, wave_value
):
    delta_x = point_x[:, None] - source_x[None, :]
    delta_y = point_y[:, None] - source_y[None, :]
    distance = jnp.sqrt(delta_x * delta_x + delta_y * delta_y + (src_depth * src_depth)[None, :])
    lid_first = jnp.where(region == 1, lid_table[1, 0], lid_table[0, 0])
    lid_second = jnp.where(region == 1, lid_table[1, 1], lid_table[0, 1])
    factor = jnp.where(src_label[None, :] == 1, lid_second[:, None], lid_first[:, None])
    amplitude = factor * jnp.exp(wave_value * src_depth)[None, :] / distance
    phase_angle = wave_value * distance
    return (
        (amplitude * jnp.cos(phase_angle)).astype(jnp.bfloat16),
        (amplitude * jnp.sin(phase_angle)).astype(jnp.bfloat16),
    )


def col_sum_to_columns(partial, offset=None):
    n_col = lax.axis_size("col")
    n_row = lax.axis_size("row")
    parts, rows, right = partial.shape
    piece = rows // n_col
    split = partial.reshape(parts, n_col, piece, right).transpose(1, 0, 2, 3)
    summed = lax.all_to_all(split, "col", 0, 0, tiled=True).sum(0)
    if offset is not None:
        start = lax.axis_index("col") * piece
        summed = lax.dynamic_slice_in_dim(offset, start, piece, 1) - summed
    spread = jnp.broadcast_to(summed[None], (n_row,) + summed.shape)
    gathered = lax.all_to_all(spread, "row", 0, 0, tiled=True)
    paired = gathered.reshape(n_col, n_row // n_col, parts, piece, right)
    moved = lax.all_to_all(paired, "col", 0, 0, tiled=True)
    return moved.transpose(2, 1, 0, 3, 4).reshape(parts, (n_row // n_col) * rows, right)


def per_device(
    inv_top,
    inv_bottom,
    lower_panel,
    rhs_top,
    rhs_bottom,
    source_xy,
    source_depth,
    body_label,
    field_xy,
    region_label,
    lid_table,
    wave_number,
):
    n_col = lax.axis_size("col")
    top_solved = col_sum_to_columns(complex_product(inv_top, rhs_top))
    remainder_cols = col_sum_to_columns(complex_product(lower_panel, top_solved), rhs_bottom)
    bottom_solved = col_sum_to_columns(complex_product(inv_bottom, remainder_cols))
    strengths = jnp.stack([top_solved, bottom_solved])
    weights = strengths.astype(jnp.bfloat16)
    right_count = weights.shape[3]
    src_real = weights[:, 0].reshape(-1, right_count)
    src_imag = weights[:, 1].reshape(-1, right_count)
    stacked = jnp.concatenate(
        [
            jnp.concatenate([src_real, src_imag], axis=1),
            jnp.concatenate([-src_imag, src_real], axis=1),
        ],
        axis=0,
    )
    source_x = source_xy[0].reshape(-1)
    source_y = source_xy[1].reshape(-1)
    src_depth = source_depth.reshape(-1)
    src_label = body_label.reshape(-1)
    wave_value = wave_number[0]

    tile_real, tile_imag = green_tile(
        field_xy[0],
        field_xy[1],
        region_label,
        source_x,
        source_y,
        src_depth,
        src_label,
        lid_table,
        wave_value,
    )
    tiles = lax.optimization_barrier(jnp.concatenate([tile_real, tile_imag], axis=1))
    result = jnp.dot(tiles, stacked, preferred_element_type=jnp.float32)
    field_rows = result.shape[0]
    out_rows = field_rows // n_col
    split = result.reshape(n_col, out_rows, 2, right_count)
    elevation = lax.all_to_all(split, "col", 0, 0, tiled=True).sum(0)
    return (strengths, elevation)


def solution(mesh):
    in_specs = (
        P(None, "row", "col"),
        P(None, "row", "col"),
        P(None, "row", "col"),
        P(None, "col", None),
        P(None, "row", None),
        P(None, None, "col"),
        P(None, "col"),
        P(None, "col"),
        P(None, "row"),
        P("row"),
        P(),
        P(),
    )
    out_specs = (P(None, None, "col", None), P(("row", "col"), None, None))
    return jax.shard_map(
        per_device, mesh=mesh, in_specs=in_specs, out_specs=out_specs, check_vma=False
    )
```

```python
import jax
import jax.numpy as jnp
from jax import lax
from jax.sharding import Mesh, PartitionSpec as P


def complex_product(matrix, vector):
    highest = lax.Precision.HIGHEST
    real_part = jnp.dot(
        matrix[0], vector[0], precision=highest, preferred_element_type=jnp.float32
    ) - jnp.dot(matrix[1], vector[1], precision=highest, preferred_element_type=jnp.float32)
    imag_part = jnp.dot(
        matrix[0], vector[1], precision=highest, preferred_element_type=jnp.float32
    ) + jnp.dot(matrix[1], vector[0], precision=highest, preferred_element_type=jnp.float32)
    return jnp.stack([real_part, imag_part])


def green_tile(
    point_x, point_y, region, source_x, source_y, src_depth, src_label, lid_table, wave_value
):
    delta_x = point_x[:, None] - source_x[None, :]
    delta_y = point_y[:, None] - source_y[None, :]
    distance = jnp.sqrt(delta_x * delta_x + delta_y * delta_y + (src_depth * src_depth)[None, :])
    lid_first = jnp.where(region == 1, lid_table[1, 0], lid_table[0, 0])
    lid_second = jnp.where(region == 1, lid_table[1, 1], lid_table[0, 1])
    factor = jnp.where(src_label[None, :] == 1, lid_second[:, None], lid_first[:, None])
    amplitude = factor * jnp.exp(wave_value * src_depth)[None, :] / distance
    phase_angle = wave_value * distance
    return (
        (amplitude * jnp.cos(phase_angle)).astype(jnp.bfloat16),
        (amplitude * jnp.sin(phase_angle)).astype(jnp.bfloat16),
    )


def col_sum_to_columns(partial, offset=None):
    n_col = lax.axis_size("col")
    n_z = lax.axis_size("z")
    parts, rows, right = partial.shape
    piece = rows // n_col
    split = partial.reshape(parts, n_col, piece, right).transpose(1, 0, 2, 3)
    summed = lax.all_to_all(split, "col", 0, 0, tiled=True).sum(0)
    if offset is not None:
        start = lax.axis_index("col") * piece
        summed = lax.dynamic_slice_in_dim(offset, start, piece, 1) - summed
    spread = jnp.broadcast_to(summed[None], (n_z,) + summed.shape)
    gathered = lax.all_to_all(spread, "z", 0, 0, tiled=True)
    moved = lax.all_to_all(gathered, "col", 0, 0, tiled=True)
    block = moved.transpose(1, 0, 2, 3).reshape(parts, rows, right)
    other = lax.ppermute(block, "core", [(0, 1), (1, 0)])
    first_core = lax.axis_index("core") == 0
    return jnp.concatenate(
        [jnp.where(first_core, block, other), jnp.where(first_core, other, block)], axis=1
    )


def per_device(
    inv_top,
    inv_bottom,
    lower_panel,
    rhs_top,
    rhs_bottom,
    source_xy,
    source_depth,
    body_label,
    field_xy,
    region_label,
    lid_table,
    wave_number,
):
    n_col = lax.axis_size("col")
    top_solved = col_sum_to_columns(complex_product(inv_top, rhs_top))
    remainder_cols = col_sum_to_columns(complex_product(lower_panel, top_solved), rhs_bottom)
    bottom_solved = col_sum_to_columns(complex_product(inv_bottom, remainder_cols))
    strengths = jnp.stack([top_solved, bottom_solved])
    weights = strengths.astype(jnp.bfloat16)
    right_count = weights.shape[3]
    src_real = weights[:, 0].reshape(-1, right_count)
    src_imag = weights[:, 1].reshape(-1, right_count)
    stacked = jnp.concatenate(
        [
            jnp.concatenate([src_real, src_imag], axis=1),
            jnp.concatenate([-src_imag, src_real], axis=1),
        ],
        axis=0,
    )
    source_x = source_xy[0].reshape(-1)
    source_y = source_xy[1].reshape(-1)
    src_depth = source_depth.reshape(-1)
    src_label = body_label.reshape(-1)
    wave_value = wave_number[0]

    tile_real, tile_imag = green_tile(
        field_xy[0],
        field_xy[1],
        region_label,
        source_x,
        source_y,
        src_depth,
        src_label,
        lid_table,
        wave_value,
    )
    tiles = lax.optimization_barrier(jnp.concatenate([tile_real, tile_imag], axis=1))
    result = jnp.dot(tiles, stacked, preferred_element_type=jnp.float32)
    field_rows = result.shape[0]
    out_rows = field_rows // n_col
    split = result.reshape(n_col, out_rows, 2 * right_count)
    summed = lax.all_to_all(split, "col", 0, 0, tiled=True).sum(0)
    elevation = summed.reshape(out_rows, 2, right_count)
    return (strengths, elevation)


def solution(mesh):
    n_row = mesh.shape["row"]
    split_mesh = Mesh(
        mesh.devices.reshape(n_row // 2, 2, mesh.shape["col"]), ("z", "core", "col")
    )
    row = ("z", "core")
    in_specs = (
        P(None, row, "col"),
        P(None, row, "col"),
        P(None, row, "col"),
        P(None, "col", None),
        P(None, row, None),
        P(None, None, "col"),
        P(None, "col"),
        P(None, "col"),
        P(None, row),
        P(row),
        P(),
        P(),
    )
    out_specs = (P(None, None, "col", None), P(("z", "core", "col"), None, None))
    return jax.shard_map(
        per_device, mesh=split_mesh, in_specs=in_specs, out_specs=out_specs, check_vma=False
    )
```

```python
import jax
import jax.numpy as jnp
from jax import lax
from jax.sharding import Mesh, PartitionSpec as P


def complex_product(matrix, vector):
    highest = lax.Precision.HIGHEST
    real_part = jnp.dot(
        matrix[0], vector[0], precision=highest, preferred_element_type=jnp.float32
    ) - jnp.dot(matrix[1], vector[1], precision=highest, preferred_element_type=jnp.float32)
    imag_part = jnp.dot(
        matrix[0], vector[1], precision=highest, preferred_element_type=jnp.float32
    ) + jnp.dot(matrix[1], vector[0], precision=highest, preferred_element_type=jnp.float32)
    return jnp.stack([real_part, imag_part])


def green_tile(
    point_x, point_y, region, source_x, source_y, src_depth, src_label, lid_table, wave_value
):
    delta_x = point_x[:, None] - source_x[None, :]
    delta_y = point_y[:, None] - source_y[None, :]
    distance = jnp.sqrt(delta_x * delta_x + delta_y * delta_y + (src_depth * src_depth)[None, :])
    lid_first = jnp.where(region == 1, lid_table[1, 0], lid_table[0, 0])
    lid_second = jnp.where(region == 1, lid_table[1, 1], lid_table[0, 1])
    factor = jnp.where(src_label[None, :] == 1, lid_second[:, None], lid_first[:, None])
    amplitude = factor * jnp.exp(wave_value * src_depth)[None, :] / distance
    phase_angle = wave_value * distance
    return (
        (amplitude * jnp.cos(phase_angle)).astype(jnp.bfloat16),
        (amplitude * jnp.sin(phase_angle)).astype(jnp.bfloat16),
    )


def beside(step, value, work):
    if work is None:
        return step(value), None
    inputs, fn = work
    value, inputs = lax.optimization_barrier((value, inputs))
    result = step(value)
    done = fn(*inputs)
    return lax.optimization_barrier((result, done))


def col_sum_to_columns(partial, offset=None, works=(None, None, None)):
    n_col = lax.axis_size("col")
    n_z = lax.axis_size("z")
    parts, rows, right = partial.shape
    piece = rows // n_col
    outputs = []

    def col_step(value):
        return lax.all_to_all(value, "col", 0, 0, tiled=True)

    def z_step(value):
        return lax.all_to_all(value, "z", 0, 0, tiled=True)

    split = partial.reshape(parts, n_col, piece, right).transpose(1, 0, 2, 3)
    scattered, out = beside(col_step, split, works[0])
    outputs.append(out)
    summed = scattered.sum(0)
    if offset is not None:
        start = lax.axis_index("col") * piece
        summed = lax.dynamic_slice_in_dim(offset, start, piece, 1) - summed
    spread = jnp.broadcast_to(summed[None], (n_z,) + summed.shape)
    gathered, out = beside(z_step, spread, works[1])
    outputs.append(out)
    moved, out = beside(col_step, gathered, works[2])
    outputs.append(out)
    block = moved.transpose(1, 0, 2, 3).reshape(parts, rows, right)
    other = lax.ppermute(block, "core", [(0, 1), (1, 0)])
    first_core = lax.axis_index("core") == 0
    vector = jnp.concatenate(
        [jnp.where(first_core, block, other), jnp.where(first_core, other, block)], axis=1
    )
    return vector, [o for o in outputs if o is not None]


def per_device(
    inv_top,
    inv_bottom,
    lower_panel,
    rhs_top,
    rhs_bottom,
    source_xy,
    source_depth,
    body_label,
    field_xy,
    region_label,
    lid_table,
    wave_number,
):
    n_col = lax.axis_size("col")
    source_x = source_xy[0].reshape(-1)
    source_y = source_xy[1].reshape(-1)
    src_depth = source_depth.reshape(-1)
    src_label = body_label.reshape(-1)
    wave_value = wave_number[0]

    def tile_chunk(point_xy, region):
        tile_real, tile_imag = green_tile(
            point_xy[0],
            point_xy[1],
            region,
            source_x,
            source_y,
            src_depth,
            src_label,
            lid_table,
            wave_value,
        )
        return jnp.concatenate([tile_real, tile_imag], axis=1)

    field_rows = field_xy.shape[1]
    n_chunks = 6
    chunk_rows = field_rows // n_chunks
    works = [
        (
            (
                field_xy[:, i * chunk_rows : (i + 1) * chunk_rows],
                region_label[i * chunk_rows : (i + 1) * chunk_rows],
            ),
            tile_chunk,
        )
        for i in range(n_chunks)
    ]
    top_solved, tiles_a = col_sum_to_columns(
        complex_product(inv_top, rhs_top), works=(None, works[0], works[1])
    )
    remainder_cols, tiles_b = col_sum_to_columns(
        complex_product(lower_panel, top_solved), rhs_bottom, works=(works[2], works[3], None)
    )
    bottom_solved, tiles_c = col_sum_to_columns(
        complex_product(inv_bottom, remainder_cols), works=(works[4], works[5], None)
    )
    tile_chunks = tiles_a + tiles_b + tiles_c
    strengths = jnp.stack([top_solved, bottom_solved])
    weights = strengths.astype(jnp.bfloat16)
    right_count = weights.shape[3]
    src_real = weights[:, 0].reshape(-1, right_count)
    src_imag = weights[:, 1].reshape(-1, right_count)
    stacked = jnp.concatenate(
        [
            jnp.concatenate([src_real, src_imag], axis=1),
            jnp.concatenate([-src_imag, src_real], axis=1),
        ],
        axis=0,
    )
    result = jnp.concatenate(
        [jnp.dot(tiles, stacked, preferred_element_type=jnp.float32) for tiles in tile_chunks],
        axis=0,
    )
    out_rows = field_rows // n_col
    split = result.reshape(n_col, out_rows, 2 * right_count)
    summed = lax.all_to_all(split, "col", 0, 0, tiled=True).sum(0)
    elevation = summed.reshape(out_rows, 2, right_count)
    return (strengths, elevation)


def solution(mesh):
    n_row = mesh.shape["row"]
    split_mesh = Mesh(
        mesh.devices.reshape(n_row // 2, 2, mesh.shape["col"]), ("z", "core", "col")
    )
    row = ("z", "core")
    in_specs = (
        P(None, row, "col"),
        P(None, row, "col"),
        P(None, row, "col"),
        P(None, "col", None),
        P(None, row, None),
        P(None, None, "col"),
        P(None, "col"),
        P(None, "col"),
        P(None, row),
        P(row),
        P(),
        P(),
    )
    out_specs = (P(None, None, "col", None), P(("z", "core", "col"), None, None))
    return jax.shard_map(
        per_device, mesh=split_mesh, in_specs=in_specs, out_specs=out_specs, check_vma=False
    )
```

```python
import jax
import jax.numpy as jnp
from jax import lax
from jax.sharding import Mesh, PartitionSpec as P


def stacked_matrix(matrix):
    return jnp.concatenate(
        [
            jnp.concatenate([matrix[0], -matrix[1]], axis=1),
            jnp.concatenate([matrix[1], matrix[0]], axis=1),
        ],
        axis=0,
    )


def complex_product(stacked, vector):
    parts, rows, right = vector.shape
    product = jnp.dot(
        stacked,
        vector.reshape(parts * rows, right),
        precision=lax.Precision.HIGHEST,
        preferred_element_type=jnp.float32,
    )
    return product.reshape(parts, stacked.shape[0] // parts, right)


def green_tile(
    point_x, point_y, region, source_x, source_y, src_depth, src_label, lid_table, wave_value
):
    delta_x = point_x[:, None] - source_x[None, :]
    delta_y = point_y[:, None] - source_y[None, :]
    distance = jnp.sqrt(delta_x * delta_x + delta_y * delta_y + (src_depth * src_depth)[None, :])
    lid_first = jnp.where(region == 1, lid_table[1, 0], lid_table[0, 0])
    lid_second = jnp.where(region == 1, lid_table[1, 1], lid_table[0, 1])
    factor = jnp.where(src_label[None, :] == 1, lid_second[:, None], lid_first[:, None])
    amplitude = factor * jnp.exp(wave_value * src_depth)[None, :] / distance
    phase_angle = wave_value * distance
    return (
        (amplitude * jnp.cos(phase_angle)).astype(jnp.bfloat16),
        (amplitude * jnp.sin(phase_angle)).astype(jnp.bfloat16),
    )


def beside(step, value, work):
    if work is None:
        return step(value), None
    inputs, fn = work
    value, inputs = lax.optimization_barrier((value, inputs))
    result = step(value)
    done = fn(*inputs)
    return lax.optimization_barrier((result, done))


def col_sum_to_columns(partial, offset=None, works=(None, None, None)):
    n_col = lax.axis_size("col")
    n_z = lax.axis_size("z")
    parts, rows, right = partial.shape
    piece = rows // n_col
    outputs = []

    def col_step(value):
        return lax.all_to_all(value, "col", 0, 0, tiled=True)

    def z_step(value):
        return lax.all_to_all(value, "z", 0, 0, tiled=True)

    split = partial.reshape(parts, n_col, piece, right).transpose(1, 0, 2, 3)
    scattered, out = beside(col_step, split, works[0])
    outputs.append(out)
    summed = scattered.sum(0)
    if offset is not None:
        start = lax.axis_index("col") * piece
        summed = lax.dynamic_slice_in_dim(offset, start, piece, 1) - summed
    spread = jnp.broadcast_to(summed[None], (n_z,) + summed.shape)
    gathered, out = beside(z_step, spread, works[1])
    outputs.append(out)
    moved, out = beside(col_step, gathered, works[2])
    outputs.append(out)
    block = moved.transpose(1, 0, 2, 3).reshape(parts, rows, right)
    other = lax.ppermute(block, "core", [(0, 1), (1, 0)])
    first_core = lax.axis_index("core") == 0
    vector = jnp.concatenate(
        [jnp.where(first_core, block, other), jnp.where(first_core, other, block)], axis=1
    )
    return vector, [o for o in outputs if o is not None]


def per_device(
    inv_top,
    inv_bottom,
    lower_panel,
    rhs_top,
    rhs_bottom,
    source_xy,
    source_depth,
    body_label,
    field_xy,
    region_label,
    lid_table,
    wave_number,
):
    n_col = lax.axis_size("col")
    source_x = source_xy[0].reshape(-1)
    source_y = source_xy[1].reshape(-1)
    src_depth = source_depth.reshape(-1)
    src_label = body_label.reshape(-1)
    wave_value = wave_number[0]

    def tile_chunk(point_xy, region):
        tile_real, tile_imag = green_tile(
            point_xy[0],
            point_xy[1],
            region,
            source_x,
            source_y,
            src_depth,
            src_label,
            lid_table,
            wave_value,
        )
        return jnp.concatenate([tile_real, tile_imag], axis=1)

    field_rows = field_xy.shape[1]
    top_solved, tile_chunks = col_sum_to_columns(
        complex_product(stacked_matrix(inv_top), rhs_top),
        works=(None, ((field_xy, region_label), tile_chunk), None),
    )
    remainder_cols, _ = col_sum_to_columns(
        complex_product(stacked_matrix(lower_panel), top_solved), rhs_bottom
    )
    bottom_solved, _ = col_sum_to_columns(
        complex_product(stacked_matrix(inv_bottom), remainder_cols)
    )
    strengths = jnp.stack([top_solved, bottom_solved])
    weights = strengths.astype(jnp.bfloat16)
    right_count = weights.shape[3]
    src_real = weights[:, 0].reshape(-1, right_count)
    src_imag = weights[:, 1].reshape(-1, right_count)
    stacked = jnp.concatenate(
        [
            jnp.concatenate([src_real, src_imag], axis=1),
            jnp.concatenate([-src_imag, src_real], axis=1),
        ],
        axis=0,
    )
    result = jnp.concatenate(
        [jnp.dot(tiles, stacked, preferred_element_type=jnp.float32) for tiles in tile_chunks],
        axis=0,
    )
    out_rows = field_rows // n_col
    split = result.reshape(n_col, out_rows, 2 * right_count)
    summed = lax.all_to_all(split, "col", 0, 0, tiled=True).sum(0)
    elevation = summed.reshape(out_rows, 2, right_count)
    return (strengths, elevation)


def solution(mesh):
    n_row = mesh.shape["row"]
    split_mesh = Mesh(
        mesh.devices.reshape(n_row // 2, 2, mesh.shape["col"]), ("z", "core", "col")
    )
    row = ("z", "core")
    in_specs = (
        P(None, row, "col"),
        P(None, row, "col"),
        P(None, row, "col"),
        P(None, "col", None),
        P(None, row, None),
        P(None, None, "col"),
        P(None, "col"),
        P(None, "col"),
        P(None, row),
        P(row),
        P(),
        P(),
    )
    out_specs = (P(None, None, "col", None), P(("z", "core", "col"), None, None))
    return jax.shard_map(
        per_device, mesh=split_mesh, in_specs=in_specs, out_specs=out_specs, check_vma=False
    )
```

```python
import jax
import jax.numpy as jnp
from jax import lax
from jax.sharding import Mesh, PartitionSpec as P


def stacked_matrix(matrix):
    return jnp.concatenate(
        [
            jnp.concatenate([matrix[0], -matrix[1]], axis=1),
            jnp.concatenate([matrix[1], matrix[0]], axis=1),
        ],
        axis=0,
    )


def complex_product(stacked, vector):
    parts, rows, right = vector.shape
    product = jnp.dot(
        stacked,
        vector.reshape(parts * rows, right),
        precision=lax.Precision.HIGHEST,
        preferred_element_type=jnp.float32,
    )
    return product.reshape(parts, stacked.shape[0] // parts, right)


def green_tile(
    point_x, point_y, region, source_x, source_y, src_depth, src_label, lid_table, wave_value
):
    delta_x = point_x[:, None] - source_x[None, :]
    delta_y = point_y[:, None] - source_y[None, :]
    distance = jnp.sqrt(delta_x * delta_x + delta_y * delta_y + (src_depth * src_depth)[None, :])
    lid_first = jnp.where(region == 1, lid_table[1, 0], lid_table[0, 0])
    lid_second = jnp.where(region == 1, lid_table[1, 1], lid_table[0, 1])
    factor = jnp.where(src_label[None, :] == 1, lid_second[:, None], lid_first[:, None])
    amplitude = factor * jnp.exp(wave_value * src_depth)[None, :] / distance
    phase_angle = wave_value * distance
    return (
        (amplitude * jnp.cos(phase_angle)).astype(jnp.bfloat16),
        (amplitude * jnp.sin(phase_angle)).astype(jnp.bfloat16),
    )


def beside(step, value, work):
    if work is None:
        return step(value), None
    inputs, fn = work
    value, inputs = lax.optimization_barrier((value, inputs))
    result = step(value)
    done = fn(*inputs)
    return lax.optimization_barrier((result, done))


def col_sum_to_columns(partial, offset=None, works=(None, None, None)):
    n_col = lax.axis_size("col")
    n_z = lax.axis_size("z")
    parts, rows, right = partial.shape
    piece = rows // n_col
    outputs = []

    def col_step(value):
        return lax.all_to_all(value, "col", 0, 0, tiled=True)

    def z_step(value):
        return lax.all_to_all(value, "z", 0, 0, tiled=True)

    split = partial.reshape(parts, n_col, piece, right).transpose(1, 0, 2, 3)
    scattered, out = beside(col_step, split, works[0])
    outputs.append(out)
    summed = scattered.sum(0)
    if offset is not None:
        start = lax.axis_index("col") * piece
        summed = lax.dynamic_slice_in_dim(offset, start, piece, 1) - summed
    spread = jnp.broadcast_to(summed[None], (n_z,) + summed.shape)
    gathered, out = beside(z_step, spread, works[1])
    outputs.append(out)
    moved, out = beside(col_step, gathered, works[2])
    outputs.append(out)
    block = moved.transpose(1, 0, 2, 3).reshape(parts, rows, right)
    other = lax.ppermute(block, "core", [(0, 1), (1, 0)])
    first_core = lax.axis_index("core") == 0
    vector = jnp.concatenate(
        [jnp.where(first_core, block, other), jnp.where(first_core, other, block)], axis=1
    )
    return vector, [o for o in outputs if o is not None]


def per_device(
    inv_top,
    inv_bottom,
    lower_panel,
    rhs_top,
    rhs_bottom,
    source_xy,
    source_depth,
    body_label,
    field_xy,
    region_label,
    lid_table,
    wave_number,
):
    n_col = lax.axis_size("col")
    source_x = source_xy[0].reshape(-1)
    source_y = source_xy[1].reshape(-1)
    src_depth = source_depth.reshape(-1)
    src_label = body_label.reshape(-1)
    wave_value = wave_number[0]

    def tile_chunk(point_xy, region):
        tile_real, tile_imag = green_tile(
            point_xy[0],
            point_xy[1],
            region,
            source_x,
            source_y,
            src_depth,
            src_label,
            lid_table,
            wave_value,
        )
        return tile_real, tile_imag

    field_rows = field_xy.shape[1]
    n_chunks = 3
    chunk_rows = field_rows // n_chunks
    works = [
        (
            (
                field_xy[:, i * chunk_rows : (i + 1) * chunk_rows],
                region_label[i * chunk_rows : (i + 1) * chunk_rows],
            ),
            tile_chunk,
        )
        for i in range(n_chunks)
    ]
    top_solved, tiles_a = col_sum_to_columns(
        complex_product(stacked_matrix(inv_top), rhs_top), works=(None, works[0], None)
    )
    remainder_cols, tiles_b = col_sum_to_columns(
        complex_product(stacked_matrix(lower_panel), top_solved),
        rhs_bottom,
        works=(None, works[1], None),
    )
    bottom_solved, tiles_c = col_sum_to_columns(
        complex_product(stacked_matrix(inv_bottom), remainder_cols), works=(None, works[2], None)
    )
    tile_chunks = tiles_a + tiles_b + tiles_c
    strengths = jnp.stack([top_solved, bottom_solved])
    weights = strengths.astype(jnp.bfloat16)
    right_count = weights.shape[3]
    src_real = weights[:, 0].reshape(-1, right_count)
    src_imag = weights[:, 1].reshape(-1, right_count)
    for_real = jnp.concatenate([src_real, src_imag], axis=1)
    for_imag = jnp.concatenate([-src_imag, src_real], axis=1)
    result = jnp.concatenate(
        [
            jnp.dot(tile_real, for_real, preferred_element_type=jnp.float32)
            + jnp.dot(tile_imag, for_imag, preferred_element_type=jnp.float32)
            for tile_real, tile_imag in tile_chunks
        ],
        axis=0,
    )
    out_rows = field_rows // n_col
    split = result.reshape(n_col, out_rows, 2 * right_count)
    summed = lax.all_to_all(split, "col", 0, 0, tiled=True).sum(0)
    elevation = summed.reshape(out_rows, 2, right_count)
    return (strengths, elevation)


def solution(mesh):
    n_row = mesh.shape["row"]
    split_mesh = Mesh(
        mesh.devices.reshape(n_row // 2, 2, mesh.shape["col"]), ("z", "core", "col")
    )
    row = ("z", "core")
    in_specs = (
        P(None, row, "col"),
        P(None, row, "col"),
        P(None, row, "col"),
        P(None, "col", None),
        P(None, row, None),
        P(None, None, "col"),
        P(None, "col"),
        P(None, "col"),
        P(None, row),
        P(row),
        P(),
        P(),
    )
    out_specs = (P(None, None, "col", None), P(("z", "core", "col"), None, None))
    return jax.shard_map(
        per_device, mesh=split_mesh, in_specs=in_specs, out_specs=out_specs, check_vma=False
    )
```

```python
import jax
import jax.numpy as jnp
from jax import lax
from jax.sharding import Mesh, PartitionSpec as P


def stacked_matrix(matrix):
    return jnp.concatenate(
        [
            jnp.concatenate([matrix[0], -matrix[1]], axis=1),
            jnp.concatenate([matrix[1], matrix[0]], axis=1),
        ],
        axis=0,
    )


def complex_product(stacked, vector):
    parts, rows, right = vector.shape
    product = jnp.dot(
        stacked,
        vector.reshape(parts * rows, right),
        precision=lax.Precision.HIGHEST,
        preferred_element_type=jnp.float32,
    )
    return product.reshape(parts, stacked.shape[0] // parts, right)


def green_tile(point_x, point_y, lid_first, lid_second, source_x, source_y, depth_sq, depth_term, src_label, wave_value):
    delta_x = point_x[:, None] - source_x[None, :]
    delta_y = point_y[:, None] - source_y[None, :]
    distance = jnp.sqrt(delta_x * delta_x + delta_y * delta_y + depth_sq[None, :])
    factor = jnp.where(src_label[None, :] == 1, lid_second[:, None], lid_first[:, None])
    amplitude = factor * depth_term[None, :] / distance
    phase_angle = wave_value * distance
    return (
        (amplitude * jnp.cos(phase_angle)).astype(jnp.bfloat16),
        (amplitude * jnp.sin(phase_angle)).astype(jnp.bfloat16),
    )


def beside(step, value, work):
    if work is None:
        return step(value), None
    inputs, fn = work
    value, inputs = lax.optimization_barrier((value, inputs))
    result = step(value)
    done = fn(*inputs)
    return lax.optimization_barrier((result, done))


def col_sum_to_columns(partial, offset=None, works=(None, None, None)):
    n_col = lax.axis_size("col")
    n_z = lax.axis_size("z")
    parts, rows, right = partial.shape
    piece = rows // n_col
    outputs = []

    def col_step(value):
        return lax.all_to_all(value, "col", 0, 0, tiled=True)

    def z_step(value):
        return lax.all_to_all(value, "z", 0, 0, tiled=True)

    split = partial.reshape(parts, n_col, piece, right).transpose(1, 0, 2, 3)
    scattered, out = beside(col_step, split, works[0])
    outputs.append(out)
    summed = scattered.sum(0)
    if offset is not None:
        start = lax.axis_index("col") * piece
        summed = lax.dynamic_slice_in_dim(offset, start, piece, 1) - summed
    spread = jnp.broadcast_to(summed[None], (n_z,) + summed.shape)
    gathered, out = beside(z_step, spread, works[1])
    outputs.append(out)
    moved, out = beside(col_step, gathered, works[2])
    outputs.append(out)
    block = moved.transpose(1, 0, 2, 3).reshape(parts, rows, right)
    other = lax.ppermute(block, "core", [(0, 1), (1, 0)])
    first_core = lax.axis_index("core") == 0
    vector = jnp.concatenate(
        [jnp.where(first_core, block, other), jnp.where(first_core, other, block)], axis=1
    )
    return vector, [o for o in outputs if o is not None]


def per_device(
    inv_top,
    inv_bottom,
    lower_panel,
    rhs_top,
    rhs_bottom,
    source_xy,
    source_depth,
    body_label,
    field_xy,
    region_label,
    lid_table,
    wave_number,
):
    n_col = lax.axis_size("col")
    source_x = source_xy[0].reshape(-1)
    source_y = source_xy[1].reshape(-1)
    src_depth = source_depth.reshape(-1)
    src_label = body_label.reshape(-1)
    wave_value = wave_number[0]

    depth_sq = src_depth * src_depth
    depth_term = jnp.exp(wave_value * src_depth)
    lid_first = jnp.where(region_label == 1, lid_table[1, 0], lid_table[0, 0])
    lid_second = jnp.where(region_label == 1, lid_table[1, 1], lid_table[0, 1])

    def tile_chunk(point_xy, first, second):
        return green_tile(
            point_xy[0],
            point_xy[1],
            first,
            second,
            source_x,
            source_y,
            depth_sq,
            depth_term,
            src_label,
            wave_value,
        )

    field_rows = field_xy.shape[1]
    n_chunks = 6
    chunk_rows = field_rows // n_chunks
    works = [
        (
            (
                field_xy[:, i * chunk_rows : (i + 1) * chunk_rows],
                lid_first[i * chunk_rows : (i + 1) * chunk_rows],
                lid_second[i * chunk_rows : (i + 1) * chunk_rows],
            ),
            tile_chunk,
        )
        for i in range(n_chunks)
    ]
    top_solved, tiles_a = col_sum_to_columns(
        complex_product(stacked_matrix(inv_top), rhs_top), works=(works[0], None, works[1])
    )
    remainder_cols, tiles_b = col_sum_to_columns(
        complex_product(stacked_matrix(lower_panel), top_solved),
        rhs_bottom,
        works=(works[2], None, works[3]),
    )
    bottom_solved, tiles_c = col_sum_to_columns(
        complex_product(stacked_matrix(inv_bottom), remainder_cols),
        works=(works[4], None, works[5]),
    )
    tile_chunks = tiles_a + tiles_b + tiles_c
    strengths = jnp.stack([top_solved, bottom_solved])
    weights = strengths.astype(jnp.bfloat16)
    right_count = weights.shape[3]
    src_real = weights[:, 0].reshape(-1, right_count)
    src_imag = weights[:, 1].reshape(-1, right_count)
    for_real = jnp.concatenate([src_real, src_imag], axis=1)
    for_imag = jnp.concatenate([-src_imag, src_real], axis=1)
    result = jnp.concatenate(
        [
            jnp.dot(tile_real, for_real, preferred_element_type=jnp.float32)
            + jnp.dot(tile_imag, for_imag, preferred_element_type=jnp.float32)
            for tile_real, tile_imag in tile_chunks
        ],
        axis=0,
    )
    out_rows = field_rows // n_col
    split = result.reshape(n_col, out_rows, 2 * right_count)
    summed = lax.all_to_all(split, "col", 0, 0, tiled=True).sum(0)
    elevation = summed.reshape(out_rows, 2, right_count)
    return (strengths, elevation)


def solution(mesh):
    n_row = mesh.shape["row"]
    split_mesh = Mesh(
        mesh.devices.reshape(n_row // 2, 2, mesh.shape["col"]), ("z", "core", "col")
    )
    row = ("z", "core")
    in_specs = (
        P(None, row, "col"),
        P(None, row, "col"),
        P(None, row, "col"),
        P(None, "col", None),
        P(None, row, None),
        P(None, None, "col"),
        P(None, "col"),
        P(None, "col"),
        P(None, row),
        P(row),
        P(),
        P(),
    )
    out_specs = (P(None, None, "col", None), P(("z", "core", "col"), None, None))
    return jax.shard_map(
        per_device, mesh=split_mesh, in_specs=in_specs, out_specs=out_specs, check_vma=False
    )
```

```python
import jax
import jax.numpy as jnp
from jax import lax
from jax.sharding import Mesh, PartitionSpec as P


def stacked_matrix(matrix):
    return jnp.concatenate(
        [
            jnp.concatenate([matrix[0], -matrix[1]], axis=1),
            jnp.concatenate([matrix[1], matrix[0]], axis=1),
        ],
        axis=0,
    )


def complex_product(stacked, vector):
    parts, rows, right = vector.shape
    product = jnp.dot(
        stacked,
        vector.reshape(parts * rows, right),
        precision=lax.Precision.HIGHEST,
        preferred_element_type=jnp.float32,
    )
    return product.reshape(parts, stacked.shape[0] // parts, right)


def green_tile(point_x, point_y, lid_first, lid_second, source_x, source_y, depth_sq, depth_term, src_label, wave_value):
    delta_x = point_x[:, None] - source_x[None, :]
    delta_y = point_y[:, None] - source_y[None, :]
    distance = jnp.sqrt(delta_x * delta_x + delta_y * delta_y + depth_sq[None, :])
    factor = jnp.where(src_label[None, :] == 1, lid_second[:, None], lid_first[:, None])
    amplitude = factor * depth_term[None, :] / distance
    phase_angle = wave_value * distance
    return (
        (amplitude * jnp.cos(phase_angle)).astype(jnp.bfloat16),
        (amplitude * jnp.sin(phase_angle)).astype(jnp.bfloat16),
    )


def beside(step, value, work):
    if work is None:
        return step(value), None
    inputs, fn = work
    value, inputs = lax.optimization_barrier((value, inputs))
    result = step(value)
    done = fn(*inputs)
    return lax.optimization_barrier((result, done))


def col_sum_to_columns(partial, offset=None, works=(None, None, None)):
    n_col = lax.axis_size("col")
    n_z = lax.axis_size("z")
    parts, rows, right = partial.shape
    piece = rows // n_col
    outputs = []

    def col_step(value):
        return lax.all_to_all(value, "col", 0, 0, tiled=True)

    def z_step(value):
        return lax.all_to_all(value, "z", 0, 0, tiled=True)

    split = partial.reshape(parts, n_col, piece, right).transpose(1, 0, 2, 3)
    scattered, out = beside(col_step, split, works[0])
    outputs.append(out)
    summed = scattered.sum(0)
    if offset is not None:
        start = lax.axis_index("col") * piece
        summed = lax.dynamic_slice_in_dim(offset, start, piece, 1) - summed
    spread = jnp.broadcast_to(summed[None], (n_z,) + summed.shape)
    gathered, out = beside(z_step, spread, works[1])
    outputs.append(out)
    moved, out = beside(col_step, gathered, works[2])
    outputs.append(out)
    block = moved.transpose(1, 0, 2, 3).reshape(parts, rows, right)
    other = lax.ppermute(block, "core", [(0, 1), (1, 0)])
    first_core = lax.axis_index("core") == 0
    vector = jnp.concatenate(
        [jnp.where(first_core, block, other), jnp.where(first_core, other, block)], axis=1
    )
    return vector, [o for o in outputs if o is not None]


def col_sum_to_rows(partial, offset, work, gather_work):
    n_col = lax.axis_size("col")
    parts, rows, right = partial.shape
    piece = rows // n_col
    split = partial.reshape(parts, n_col, piece, right).transpose(1, 0, 2, 3)
    scattered, done = beside(
        lambda value: lax.all_to_all(value, "col", 0, 0, tiled=True), split, work
    )
    start = lax.axis_index("col") * piece
    summed = lax.dynamic_slice_in_dim(offset, start, piece, 1) - scattered.sum(0)
    spread = jnp.broadcast_to(summed[None], (n_col,) + summed.shape)
    gathered, gather_done = beside(
        lambda value: lax.all_to_all(value, "col", 0, 0, tiled=True), spread, gather_work
    )
    return gathered.transpose(1, 0, 2, 3).reshape(parts, rows, right), [done, gather_done]


def row_sum(partial, works):
    n_z = lax.axis_size("z")
    parts, rows, right = partial.shape
    piece = rows // n_z
    chip = partial + lax.ppermute(partial, "core", [(0, 1), (1, 0)])
    split = chip.reshape(parts, n_z, piece, right).transpose(1, 0, 2, 3)
    def z_step(value):
        return lax.all_to_all(value, "z", 0, 0, tiled=True)

    scattered, first_done = beside(z_step, split, works[0])
    summed = scattered.sum(0)
    spread = jnp.broadcast_to(summed[None], (n_z,) + summed.shape)
    gathered, second_done = beside(z_step, spread, works[1])
    return gathered.transpose(1, 0, 2, 3).reshape(parts, rows, right), [first_done, second_done]


def rows_of_column_block(block):
    n_z = lax.axis_size("z")
    n_col = lax.axis_size("col")
    parts, rows, _ = block.shape
    core = lax.axis_index("core")
    halves = block.reshape(parts, rows, 2, rows)
    own_half = jnp.where(core == 0, halves[:, :, 0], halves[:, :, 1])
    other_half = jnp.where(core == 0, halves[:, :, 1], halves[:, :, 0])

    def index(z, k, c):
        return (z * 2 + k) * n_col + c

    same = [(index(z, k, c), index(c, k, z)) for z in range(n_z) for k in range(2) for c in range(n_col)]
    flip = [(index(z, k, c), index(c, 1 - k, z)) for z in range(n_z) for k in range(2) for c in range(n_col)]
    axes = ("z", "core", "col")
    from_same = lax.ppermute(own_half, axes, same)
    from_flip = lax.ppermute(other_half, axes, flip)
    first = jnp.where(core == 0, from_same, from_flip)
    second = jnp.where(core == 0, from_flip, from_same)
    return jnp.concatenate([first, second], axis=1)


def per_device(
    inv_top,
    inv_bottom,
    lower_panel,
    rhs_top,
    rhs_bottom,
    source_xy,
    source_depth,
    body_label,
    field_xy,
    region_label,
    lid_table,
    wave_number,
):
    n_col = lax.axis_size("col")
    source_x = source_xy[0].reshape(-1)
    source_y = source_xy[1].reshape(-1)
    src_depth = source_depth.reshape(-1)
    src_label = body_label.reshape(-1)
    wave_value = wave_number[0]

    depth_sq = src_depth * src_depth
    depth_term = jnp.exp(wave_value * src_depth)
    lid_first = jnp.where(region_label == 1, lid_table[1, 0], lid_table[0, 0])
    lid_second = jnp.where(region_label == 1, lid_table[1, 1], lid_table[0, 1])

    def tile_chunk(point_xy, first, second):
        return green_tile(
            point_xy[0],
            point_xy[1],
            first,
            second,
            source_x,
            source_y,
            depth_sq,
            depth_term,
            src_label,
            wave_value,
        )

    field_rows = field_xy.shape[1]
    n_chunks = 6
    chunk_rows = field_rows // n_chunks
    works = [
        (
            (
                field_xy[:, i * chunk_rows : (i + 1) * chunk_rows],
                lid_first[i * chunk_rows : (i + 1) * chunk_rows],
                lid_second[i * chunk_rows : (i + 1) * chunk_rows],
            ),
            tile_chunk,
        )
        for i in range(n_chunks)
    ]
    top_solved, tiles_a = col_sum_to_columns(
        complex_product(stacked_matrix(inv_top), rhs_top), works=(works[0], None, works[1])
    )
    bottom_moved = stacked_matrix(rows_of_column_block(inv_bottom))
    remainder_rows, tiles_b = col_sum_to_rows(
        complex_product(stacked_matrix(lower_panel), top_solved), rhs_bottom, works[2], works[3]
    )
    bottom_solved, tiles_c = row_sum(
        complex_product(bottom_moved, remainder_rows), (works[4], works[5])
    )
    tile_chunks = tiles_a + tiles_b + tiles_c
    strengths = jnp.stack([top_solved, bottom_solved])
    weights = strengths.astype(jnp.bfloat16)
    right_count = weights.shape[3]
    src_real = weights[:, 0].reshape(-1, right_count)
    src_imag = weights[:, 1].reshape(-1, right_count)
    for_real = jnp.concatenate([src_real, src_imag], axis=1)
    for_imag = jnp.concatenate([-src_imag, src_real], axis=1)
    result = jnp.concatenate(
        [
            jnp.dot(tile_real, for_real, preferred_element_type=jnp.float32)
            + jnp.dot(tile_imag, for_imag, preferred_element_type=jnp.float32)
            for tile_real, tile_imag in tile_chunks
        ],
        axis=0,
    )
    out_rows = field_rows // n_col
    split = result.reshape(n_col, out_rows, 2 * right_count)
    summed = lax.all_to_all(split, "col", 0, 0, tiled=True).sum(0)
    elevation = summed.reshape(out_rows, 2, right_count)
    return (strengths, elevation)


def solution(mesh):
    n_row = mesh.shape["row"]
    split_mesh = Mesh(
        mesh.devices.reshape(n_row // 2, 2, mesh.shape["col"]), ("z", "core", "col")
    )
    row = ("z", "core")
    in_specs = (
        P(None, row, "col"),
        P(None, row, "col"),
        P(None, row, "col"),
        P(None, "col", None),
        P(None, row, None),
        P(None, None, "col"),
        P(None, "col"),
        P(None, "col"),
        P(None, row),
        P(row),
        P(),
        P(),
    )
    out_specs = (P(None, None, "col", None), P(("z", "core", "col"), None, None))
    return jax.shard_map(
        per_device, mesh=split_mesh, in_specs=in_specs, out_specs=out_specs, check_vma=False
    )
```

```python
import jax
import jax.numpy as jnp
from jax import lax
from jax.sharding import Mesh, PartitionSpec as P


def stacked_matrix(matrix):
    return jnp.concatenate(
        [
            jnp.concatenate([matrix[0], -matrix[1]], axis=1),
            jnp.concatenate([matrix[1], matrix[0]], axis=1),
        ],
        axis=0,
    )


def complex_product(stacked, vector):
    parts, rows, right = vector.shape
    product = jnp.dot(
        stacked,
        vector.reshape(parts * rows, right),
        precision=lax.Precision.HIGHEST,
        preferred_element_type=jnp.float32,
    )
    return product.reshape(parts, stacked.shape[0] // parts, right)


def green_tile(point_x, point_y, lid_first, lid_second, source_x, source_y, depth_sq, depth_term, src_label, wave_value):
    delta_x = point_x[:, None] - source_x[None, :]
    delta_y = point_y[:, None] - source_y[None, :]
    distance = jnp.sqrt(delta_x * delta_x + delta_y * delta_y + depth_sq[None, :])
    factor = jnp.where(src_label[None, :] == 1, lid_second[:, None], lid_first[:, None])
    amplitude = factor * depth_term[None, :] / distance
    phase_angle = wave_value * distance
    return (
        (amplitude * jnp.cos(phase_angle)).astype(jnp.bfloat16),
        (amplitude * jnp.sin(phase_angle)).astype(jnp.bfloat16),
    )


def beside(step, value, work):
    if work is None:
        return step(value), None
    inputs, fn = work
    value, inputs = lax.optimization_barrier((value, inputs))
    result = step(value)
    done = fn(*inputs)
    return lax.optimization_barrier((result, done))


def col_sum_to_columns(partial, offset=None, works=(None, None, None)):
    n_col = lax.axis_size("col")
    n_z = lax.axis_size("z")
    parts, rows, right = partial.shape
    piece = rows // n_col
    outputs = []

    def col_step(value):
        return lax.all_to_all(value, "col", 0, 0, tiled=True)

    def z_step(value):
        return lax.all_to_all(value, "z", 0, 0, tiled=True)

    split = partial.reshape(parts, n_col, piece, right).transpose(1, 0, 2, 3)
    scattered, out = beside(col_step, split, works[0])
    outputs.append(out)
    summed = scattered.sum(0)
    if offset is not None:
        start = lax.axis_index("col") * piece
        summed = lax.dynamic_slice_in_dim(offset, start, piece, 1) - summed
    spread = jnp.broadcast_to(summed[None], (n_z,) + summed.shape)
    gathered, out = beside(z_step, spread, works[1])
    outputs.append(out)
    moved, out = beside(col_step, gathered, works[2])
    outputs.append(out)
    block = moved.transpose(1, 0, 2, 3).reshape(parts, rows, right)
    other = lax.ppermute(block, "core", [(0, 1), (1, 0)])
    first_core = lax.axis_index("core") == 0
    vector = jnp.concatenate(
        [jnp.where(first_core, block, other), jnp.where(first_core, other, block)], axis=1
    )
    return vector, [o for o in outputs if o is not None]


def col_sum_to_rows(partial, offset, work, gather_work):
    n_col = lax.axis_size("col")
    parts, rows, right = partial.shape
    piece = rows // n_col
    split = partial.reshape(parts, n_col, piece, right).transpose(1, 0, 2, 3)
    scattered, done = beside(
        lambda value: lax.all_to_all(value, "col", 0, 0, tiled=True), split, work
    )
    start = lax.axis_index("col") * piece
    summed = lax.dynamic_slice_in_dim(offset, start, piece, 1) - scattered.sum(0)
    spread = jnp.broadcast_to(summed[None], (n_col,) + summed.shape)
    gathered, gather_done = beside(
        lambda value: lax.all_to_all(value, "col", 0, 0, tiled=True), spread, gather_work
    )
    return gathered.transpose(1, 0, 2, 3).reshape(parts, rows, right), [done, gather_done]


def row_sum(partial, works):
    n_z = lax.axis_size("z")
    parts, rows, right = partial.shape
    piece = rows // n_z
    chip = partial + lax.ppermute(partial, "core", [(0, 1), (1, 0)])
    split = chip.reshape(parts, n_z, piece, right).transpose(1, 0, 2, 3)
    def z_step(value):
        return lax.all_to_all(value, "z", 0, 0, tiled=True)

    scattered, first_done = beside(z_step, split, works[0])
    summed = scattered.sum(0)
    spread = jnp.broadcast_to(summed[None], (n_z,) + summed.shape)
    gathered, second_done = beside(z_step, spread, works[1])
    return gathered.transpose(1, 0, 2, 3).reshape(parts, rows, right), [first_done, second_done]


def rows_of_column_block(block):
    n_z = lax.axis_size("z")
    n_col = lax.axis_size("col")
    parts, rows, _ = block.shape
    core = lax.axis_index("core")
    halves = block.reshape(parts, rows, 2, rows)
    own_half = jnp.where(core == 0, halves[:, :, 0], halves[:, :, 1])
    other_half = jnp.where(core == 0, halves[:, :, 1], halves[:, :, 0])

    def index(z, k, c):
        return (z * 2 + k) * n_col + c

    same = [(index(z, k, c), index(c, k, z)) for z in range(n_z) for k in range(2) for c in range(n_col)]
    flip = [(index(z, k, c), index(c, 1 - k, z)) for z in range(n_z) for k in range(2) for c in range(n_col)]
    axes = ("z", "core", "col")
    from_same = lax.ppermute(own_half, axes, same)
    from_flip = lax.ppermute(other_half, axes, flip)
    first = jnp.where(core == 0, from_same, from_flip)
    second = jnp.where(core == 0, from_flip, from_same)
    return jnp.concatenate([first, second], axis=1)


def per_device(
    inv_top,
    inv_bottom,
    lower_panel,
    rhs_top,
    rhs_bottom,
    source_xy,
    source_depth,
    body_label,
    field_xy,
    region_label,
    lid_table,
    wave_number,
):
    n_col = lax.axis_size("col")
    source_x = source_xy[0].reshape(-1)
    source_y = source_xy[1].reshape(-1)
    src_depth = source_depth.reshape(-1)
    src_label = body_label.reshape(-1)
    wave_value = wave_number[0]

    depth_sq = src_depth * src_depth
    depth_term = jnp.exp(wave_value * src_depth)
    lid_first = jnp.where(region_label == 1, lid_table[1, 0], lid_table[0, 0])
    lid_second = jnp.where(region_label == 1, lid_table[1, 1], lid_table[0, 1])

    def tile_chunk(point_xy, first, second):
        return green_tile(
            point_xy[0],
            point_xy[1],
            first,
            second,
            source_x,
            source_y,
            depth_sq,
            depth_term,
            src_label,
            wave_value,
        )

    field_rows = field_xy.shape[1]
    n_chunks = 6
    chunk_rows = field_rows // n_chunks
    works = [
        (
            (
                field_xy[:, i * chunk_rows : (i + 1) * chunk_rows],
                lid_first[i * chunk_rows : (i + 1) * chunk_rows],
                lid_second[i * chunk_rows : (i + 1) * chunk_rows],
            ),
            tile_chunk,
        )
        for i in range(n_chunks)
    ]
    top_solved, tiles_a = col_sum_to_columns(
        complex_product(stacked_matrix(inv_top), rhs_top), works=(works[0], None, works[1])
    )
    inv_bottom, top_solved = lax.optimization_barrier((inv_bottom, top_solved))
    bottom_moved = stacked_matrix(rows_of_column_block(inv_bottom))
    remainder_rows, tiles_b = col_sum_to_rows(
        complex_product(stacked_matrix(lower_panel), top_solved), rhs_bottom, works[2], works[3]
    )
    bottom_solved, tiles_c = row_sum(
        complex_product(bottom_moved, remainder_rows), (works[4], works[5])
    )
    tile_chunks = tiles_a + tiles_b + tiles_c
    strengths = jnp.stack([top_solved, bottom_solved])
    weights = strengths.astype(jnp.bfloat16)
    right_count = weights.shape[3]
    src_real = weights[:, 0].reshape(-1, right_count)
    src_imag = weights[:, 1].reshape(-1, right_count)
    for_real = jnp.concatenate([src_real, src_imag], axis=1)
    for_imag = jnp.concatenate([-src_imag, src_real], axis=1)
    result = jnp.concatenate(
        [
            jnp.dot(tile_real, for_real, preferred_element_type=jnp.float32)
            + jnp.dot(tile_imag, for_imag, preferred_element_type=jnp.float32)
            for tile_real, tile_imag in tile_chunks
        ],
        axis=0,
    )
    out_rows = field_rows // n_col
    split = result.reshape(n_col, out_rows, 2 * right_count)
    summed = lax.all_to_all(split, "col", 0, 0, tiled=True).sum(0)
    elevation = summed.reshape(out_rows, 2, right_count)
    return (strengths, elevation)


def solution(mesh):
    n_row = mesh.shape["row"]
    split_mesh = Mesh(
        mesh.devices.reshape(n_row // 2, 2, mesh.shape["col"]), ("z", "core", "col")
    )
    row = ("z", "core")
    in_specs = (
        P(None, row, "col"),
        P(None, row, "col"),
        P(None, row, "col"),
        P(None, "col", None),
        P(None, row, None),
        P(None, None, "col"),
        P(None, "col"),
        P(None, "col"),
        P(None, row),
        P(row),
        P(),
        P(),
    )
    out_specs = (P(None, None, "col", None), P(("z", "core", "col"), None, None))
    return jax.shard_map(
        per_device, mesh=split_mesh, in_specs=in_specs, out_specs=out_specs, check_vma=False
    )
```

```python
import jax
import jax.numpy as jnp
from jax import lax
from jax.sharding import Mesh, PartitionSpec as P


def stacked_matrix(matrix):
    return jnp.concatenate(
        [
            jnp.concatenate([matrix[0], -matrix[1]], axis=1),
            jnp.concatenate([matrix[1], matrix[0]], axis=1),
        ],
        axis=0,
    )


def complex_product(stacked, vector):
    parts, rows, right = vector.shape
    product = jnp.dot(
        stacked,
        vector.reshape(parts * rows, right),
        precision=lax.Precision.HIGHEST,
        preferred_element_type=jnp.float32,
    )
    return product.reshape(parts, stacked.shape[0] // parts, right)


def green_tile(point_x, point_y, lid_first, lid_second, source_x, source_y, depth_sq, depth_term, src_label, wave_value):
    delta_x = point_x[:, None] - source_x[None, :]
    delta_y = point_y[:, None] - source_y[None, :]
    distance = jnp.sqrt(delta_x * delta_x + delta_y * delta_y + depth_sq[None, :])
    factor = jnp.where(src_label[None, :] == 1, lid_second[:, None], lid_first[:, None])
    amplitude = factor * depth_term[None, :] / distance
    phase_angle = wave_value * distance
    return (
        (amplitude * jnp.cos(phase_angle)).astype(jnp.bfloat16),
        (amplitude * jnp.sin(phase_angle)).astype(jnp.bfloat16),
    )


def beside(step, value, work):
    if work is None:
        return step(value), None
    inputs, fn = work
    value, inputs = lax.optimization_barrier((value, inputs))
    result = step(value)
    done = fn(*inputs)
    return lax.optimization_barrier((result, done))


def col_sum_to_columns(partial, offset=None, works=(None, None, None)):
    n_col = lax.axis_size("col")
    n_z = lax.axis_size("z")
    parts, rows, right = partial.shape
    piece = rows // n_col
    outputs = []

    def col_step(value):
        return lax.all_to_all(value, "col", 0, 0, tiled=True)

    def z_step(value):
        return lax.all_to_all(value, "z", 0, 0, tiled=True)

    split = partial.reshape(parts, n_col, piece, right).transpose(1, 0, 2, 3)
    scattered, out = beside(col_step, split, works[0])
    outputs.append(out)
    summed = scattered.sum(0)
    if offset is not None:
        start = lax.axis_index("col") * piece
        summed = lax.dynamic_slice_in_dim(offset, start, piece, 1) - summed
    spread = jnp.broadcast_to(summed[None], (n_z,) + summed.shape)
    gathered, out = beside(z_step, spread, works[1])
    outputs.append(out)
    last_work = works[2](outputs) if callable(works[2]) else works[2]
    moved, out = beside(col_step, gathered, last_work)
    outputs.append(out)
    block = moved.transpose(1, 0, 2, 3).reshape(parts, rows, right)
    other = lax.ppermute(block, "core", [(0, 1), (1, 0)])
    first_core = lax.axis_index("core") == 0
    vector = jnp.concatenate(
        [jnp.where(first_core, block, other), jnp.where(first_core, other, block)], axis=1
    )
    return vector, [o for o in outputs if o is not None]


def per_device(
    inv_top,
    inv_bottom,
    lower_panel,
    rhs_top,
    rhs_bottom,
    source_xy,
    source_depth,
    body_label,
    field_xy,
    region_label,
    lid_table,
    wave_number,
):
    n_col = lax.axis_size("col")
    source_x = source_xy[0].reshape(-1)
    source_y = source_xy[1].reshape(-1)
    src_depth = source_depth.reshape(-1)
    src_label = body_label.reshape(-1)
    wave_value = wave_number[0]

    depth_sq = src_depth * src_depth
    depth_term = jnp.exp(wave_value * src_depth)
    def lids(region):
        return (
            jnp.where(region == 1, lid_table[1, 0], lid_table[0, 0]),
            jnp.where(region == 1, lid_table[1, 1], lid_table[0, 1]),
        )

    def tile_chunk(point_xy, first, second):
        return green_tile(
            point_xy[0],
            point_xy[1],
            first,
            second,
            source_x,
            source_y,
            depth_sq,
            depth_term,
            src_label,
            wave_value,
        )

    field_rows = field_xy.shape[1]
    n_chunks = 6
    chunk_rows = field_rows // n_chunks
    def first_chunk(point_xy, region):
        lid_first, lid_second = lids(region)
        tile = tile_chunk(point_xy[:, :chunk_rows], lid_first[:chunk_rows], lid_second[:chunk_rows])
        return tile, (lid_first, lid_second)

    top_partial = complex_product(stacked_matrix(inv_top), rhs_top)
    works = [((field_xy, region_label), first_chunk)] + [None] * (n_chunks - 1)

    def chunk_work(i, lid_pair):
        rows = slice(i * chunk_rows, (i + 1) * chunk_rows)
        return ((field_xy[:, rows], lid_pair[0][rows], lid_pair[1][rows]), tile_chunk)

    top_solved, tiles_a = col_sum_to_columns(
        top_partial, works=(works[0], None, lambda done: chunk_work(1, done[0][1]))
    )
    lid_pair = tiles_a[0][1]
    tiles_a = [tiles_a[0][0], tiles_a[1]]
    works = [None] + [chunk_work(i, lid_pair) for i in range(1, n_chunks)]
    remainder_cols, tiles_b = col_sum_to_columns(
        complex_product(stacked_matrix(lower_panel), top_solved),
        rhs_bottom,
        works=(works[2], None, works[3]),
    )
    bottom_solved, tiles_c = col_sum_to_columns(
        complex_product(stacked_matrix(inv_bottom), remainder_cols),
        works=(works[4], None, works[5]),
    )
    tile_chunks = tiles_a + tiles_b + tiles_c
    strengths = jnp.stack([top_solved, bottom_solved])
    weights = strengths.astype(jnp.bfloat16)
    right_count = weights.shape[3]
    src_real = weights[:, 0].reshape(-1, right_count)
    src_imag = weights[:, 1].reshape(-1, right_count)
    for_real = jnp.concatenate([src_real, src_imag], axis=1)
    for_imag = jnp.concatenate([-src_imag, src_real], axis=1)
    result = jnp.concatenate(
        [
            jnp.dot(tile_real, for_real, preferred_element_type=jnp.float32)
            + jnp.dot(tile_imag, for_imag, preferred_element_type=jnp.float32)
            for tile_real, tile_imag in tile_chunks
        ],
        axis=0,
    )
    out_rows = field_rows // n_col
    split = result.reshape(n_col, out_rows, 2 * right_count)
    summed = lax.all_to_all(split, "col", 0, 0, tiled=True).sum(0)
    elevation = summed.reshape(out_rows, 2, right_count)
    return (strengths, elevation)


def solution(mesh):
    n_row = mesh.shape["row"]
    split_mesh = Mesh(
        mesh.devices.reshape(n_row // 2, 2, mesh.shape["col"]), ("z", "core", "col")
    )
    row = ("z", "core")
    in_specs = (
        P(None, row, "col"),
        P(None, row, "col"),
        P(None, row, "col"),
        P(None, "col", None),
        P(None, row, None),
        P(None, None, "col"),
        P(None, "col"),
        P(None, "col"),
        P(None, row),
        P(row),
        P(),
        P(),
    )
    out_specs = (P(None, None, "col", None), P(("z", "core", "col"), None, None))
    return jax.shard_map(
        per_device, mesh=split_mesh, in_specs=in_specs, out_specs=out_specs, check_vma=False
    )
```

```python
import jax
import jax.numpy as jnp
from jax import lax
from jax.sharding import Mesh, PartitionSpec as P


def stacked_matrix(matrix):
    return jnp.concatenate(
        [
            jnp.concatenate([matrix[0], -matrix[1]], axis=1),
            jnp.concatenate([matrix[1], matrix[0]], axis=1),
        ],
        axis=0,
    )


def complex_product(stacked, vector):
    parts, rows, right = vector.shape
    product = jnp.dot(
        stacked,
        vector.reshape(parts * rows, right),
        precision=lax.Precision.HIGHEST,
        preferred_element_type=jnp.float32,
    )
    return product.reshape(parts, stacked.shape[0] // parts, right)


def green_tile(point_x, point_y, lid_first, lid_second, source_x, source_y, depth_sq, depth_term, src_label, wave_value):
    delta_x = point_x[:, None] - source_x[None, :]
    delta_y = point_y[:, None] - source_y[None, :]
    distance = jnp.sqrt(delta_x * delta_x + delta_y * delta_y + depth_sq[None, :])
    factor = jnp.where(src_label[None, :] == 1, lid_second[:, None], lid_first[:, None])
    amplitude = factor * depth_term[None, :] / distance
    phase_angle = wave_value * distance
    return (
        (amplitude * jnp.cos(phase_angle)).astype(jnp.bfloat16),
        (amplitude * jnp.sin(phase_angle)).astype(jnp.bfloat16),
    )


def beside(step, value, work):
    if work is None:
        return step(value), None
    inputs, fn = work
    value, inputs = lax.optimization_barrier((value, inputs))
    result = step(value)
    done = fn(*inputs)
    return lax.optimization_barrier((result, done))


def col_sum_to_columns(partial, offset=None, works=(None, None, None)):
    n_col = lax.axis_size("col")
    n_z = lax.axis_size("z")
    parts, rows, right = partial.shape
    piece = rows // n_col
    outputs = []

    def col_step(value):
        return lax.all_to_all(value, "col", 0, 0, tiled=True)

    def z_step(value):
        return lax.all_to_all(value, "z", 0, 0, tiled=True)

    split = partial.reshape(parts, n_col, piece, right).transpose(1, 0, 2, 3)
    scattered, out = beside(col_step, split, works[0])
    outputs.append(out)
    summed = scattered.sum(0)
    if offset is not None:
        start = lax.axis_index("col") * piece
        summed = lax.dynamic_slice_in_dim(offset, start, piece, 1) - summed
    spread = jnp.broadcast_to(summed[None], (n_z,) + summed.shape)
    middle_work = works[1](outputs) if callable(works[1]) else works[1]
    gathered, out = beside(z_step, spread, middle_work)
    outputs.append(out)
    last_work = works[2](outputs) if callable(works[2]) else works[2]
    moved, out = beside(col_step, gathered, last_work)
    outputs.append(out)
    block = moved.transpose(1, 0, 2, 3).reshape(parts, rows, right)
    other = lax.ppermute(block, "core", [(0, 1), (1, 0)])
    first_core = lax.axis_index("core") == 0
    vector = jnp.concatenate(
        [jnp.where(first_core, block, other), jnp.where(first_core, other, block)], axis=1
    )
    return vector, [o for o in outputs if o is not None]


def per_device(
    inv_top,
    inv_bottom,
    lower_panel,
    rhs_top,
    rhs_bottom,
    source_xy,
    source_depth,
    body_label,
    field_xy,
    region_label,
    lid_table,
    wave_number,
):
    n_col = lax.axis_size("col")
    source_x = source_xy[0].reshape(-1)
    source_y = source_xy[1].reshape(-1)
    src_depth = source_depth.reshape(-1)
    src_label = body_label.reshape(-1)
    wave_value = wave_number[0]

    depth_sq = src_depth * src_depth
    depth_term = jnp.exp(wave_value * src_depth)
    def lids(region):
        return (
            jnp.where(region == 1, lid_table[1, 0], lid_table[0, 0]),
            jnp.where(region == 1, lid_table[1, 1], lid_table[0, 1]),
        )

    def tile_chunk(point_xy, first, second):
        return green_tile(
            point_xy[0],
            point_xy[1],
            first,
            second,
            source_x,
            source_y,
            depth_sq,
            depth_term,
            src_label,
            wave_value,
        )

    field_rows = field_xy.shape[1]
    n_chunks = 6
    chunk_rows = field_rows // n_chunks
    def first_chunk(point_xy, region):
        lid_first, lid_second = lids(region)
        tile = tile_chunk(point_xy[:, :chunk_rows], lid_first[:chunk_rows], lid_second[:chunk_rows])
        return tile, (lid_first, lid_second)

    top_partial = complex_product(stacked_matrix(inv_top), rhs_top)
    works = [((field_xy, region_label), first_chunk)] + [None] * (n_chunks - 1)

    def chunk_work(first, last, lid_pair):
        rows = slice(first * chunk_rows, last * chunk_rows)
        return ((field_xy[:, rows], lid_pair[0][rows], lid_pair[1][rows]), tile_chunk)

    top_solved, tiles_a = col_sum_to_columns(
        top_partial,
        works=(
            works[0],
            lambda done: chunk_work(1, 3, done[0][1]),
            lambda done: chunk_work(3, 4, done[0][1]),
        ),
    )
    lid_pair = tiles_a[0][1]
    tiles_a = [tiles_a[0][0]] + tiles_a[1:]
    remainder_cols, tiles_b = col_sum_to_columns(
        complex_product(stacked_matrix(lower_panel), top_solved),
        rhs_bottom,
        works=(chunk_work(4, 5, lid_pair), None, chunk_work(5, 6, lid_pair)),
    )
    bottom_solved, tiles_c = col_sum_to_columns(
        complex_product(stacked_matrix(inv_bottom), remainder_cols)
    )
    tile_chunks = tiles_a + tiles_b + tiles_c
    strengths = jnp.stack([top_solved, bottom_solved])
    weights = strengths.astype(jnp.bfloat16)
    right_count = weights.shape[3]
    src_real = weights[:, 0].reshape(-1, right_count)
    src_imag = weights[:, 1].reshape(-1, right_count)
    for_real = jnp.concatenate([src_real, src_imag], axis=1)
    for_imag = jnp.concatenate([-src_imag, src_real], axis=1)
    result = jnp.concatenate(
        [
            jnp.dot(tile_real, for_real, preferred_element_type=jnp.float32)
            + jnp.dot(tile_imag, for_imag, preferred_element_type=jnp.float32)
            for tile_real, tile_imag in tile_chunks
        ],
        axis=0,
    )
    out_rows = field_rows // n_col
    split = result.reshape(n_col, out_rows, 2 * right_count)
    summed = lax.all_to_all(split, "col", 0, 0, tiled=True).sum(0)
    elevation = summed.reshape(out_rows, 2, right_count)
    return (strengths, elevation)


def solution(mesh):
    n_row = mesh.shape["row"]
    split_mesh = Mesh(
        mesh.devices.reshape(n_row // 2, 2, mesh.shape["col"]), ("z", "core", "col")
    )
    row = ("z", "core")
    in_specs = (
        P(None, row, "col"),
        P(None, row, "col"),
        P(None, row, "col"),
        P(None, "col", None),
        P(None, row, None),
        P(None, None, "col"),
        P(None, "col"),
        P(None, "col"),
        P(None, row),
        P(row),
        P(),
        P(),
    )
    out_specs = (P(None, None, "col", None), P(("z", "core", "col"), None, None))
    return jax.shard_map(
        per_device, mesh=split_mesh, in_specs=in_specs, out_specs=out_specs, check_vma=False
    )
```

```python
import jax
import jax.numpy as jnp
from jax import lax
from jax.sharding import Mesh, PartitionSpec as P


def stacked_matrix(matrix):
    return jnp.concatenate(
        [
            jnp.concatenate([matrix[0], -matrix[1]], axis=1),
            jnp.concatenate([matrix[1], matrix[0]], axis=1),
        ],
        axis=0,
    )


def complex_product(stacked, vector):
    parts, rows, right = vector.shape
    product = jnp.dot(
        stacked,
        vector.reshape(parts * rows, right),
        precision=lax.Precision.HIGHEST,
        preferred_element_type=jnp.float32,
    )
    return product.reshape(parts, stacked.shape[0] // parts, right)


def green_tile(point_x, point_y, lid_first, lid_second, source_x, source_y, depth_sq, depth_term, src_label, wave_value):
    delta_x = point_x[:, None] - source_x[None, :]
    delta_y = point_y[:, None] - source_y[None, :]
    distance = jnp.sqrt(delta_x * delta_x + delta_y * delta_y + depth_sq[None, :])
    factor = jnp.where(src_label[None, :] == 1, lid_second[:, None], lid_first[:, None])
    amplitude = factor * depth_term[None, :] / distance
    phase_angle = wave_value * distance
    return (
        (amplitude * jnp.cos(phase_angle)).astype(jnp.bfloat16),
        (amplitude * jnp.sin(phase_angle)).astype(jnp.bfloat16),
    )


def beside(step, value, work):
    if work is None:
        return step(value), None
    inputs, fn = work
    value, inputs = lax.optimization_barrier((value, inputs))
    result = step(value)
    done = fn(*inputs)
    return lax.optimization_barrier((result, done))


def col_sum_to_columns(partial, offset=None, works=(None, None, None)):
    n_col = lax.axis_size("col")
    n_z = lax.axis_size("z")
    parts, rows, right = partial.shape
    piece = rows // n_col
    outputs = []

    def col_step(value):
        return lax.all_to_all(value, "col", 0, 0, tiled=True)

    def z_step(value):
        return lax.all_to_all(value, "z", 0, 0, tiled=True)

    split = partial.reshape(parts, n_col, piece, right).transpose(1, 0, 2, 3)
    scattered, out = beside(col_step, split, works[0])
    outputs.append(out)
    summed = scattered.sum(0)
    if offset is not None:
        start = lax.axis_index("col") * piece
        summed = lax.dynamic_slice_in_dim(offset, start, piece, 1) - summed
    spread = jnp.broadcast_to(summed[None], (n_z,) + summed.shape)
    gathered, out = beside(z_step, spread, works[1])
    outputs.append(out)
    last_work = works[2](outputs) if callable(works[2]) else works[2]
    moved, out = beside(col_step, gathered, last_work)
    outputs.append(out)
    block = moved.transpose(1, 0, 2, 3).reshape(parts, rows, right)
    other = lax.ppermute(block, "core", [(0, 1), (1, 0)])
    first_core = lax.axis_index("core") == 0
    vector = jnp.concatenate(
        [jnp.where(first_core, block, other), jnp.where(first_core, other, block)], axis=1
    )
    return vector, [o for o in outputs if o is not None]


def per_device(
    inv_top,
    inv_bottom,
    lower_panel,
    rhs_top,
    rhs_bottom,
    source_xy,
    source_depth,
    body_label,
    field_xy,
    region_label,
    lid_table,
    wave_number,
):
    n_col = lax.axis_size("col")
    source_x = source_xy[0].reshape(-1)
    source_y = source_xy[1].reshape(-1)
    src_depth = source_depth.reshape(-1)
    src_label = body_label.reshape(-1)
    wave_value = wave_number[0]

    depth_sq = src_depth * src_depth
    depth_term = jnp.exp(wave_value * src_depth)
    def lids(region):
        return (
            jnp.where(region == 1, lid_table[1, 0], lid_table[0, 0]),
            jnp.where(region == 1, lid_table[1, 1], lid_table[0, 1]),
        )

    def tile_chunk(point_xy, first, second):
        return green_tile(
            point_xy[0],
            point_xy[1],
            first,
            second,
            source_x,
            source_y,
            depth_sq,
            depth_term,
            src_label,
            wave_value,
        )

    field_rows = field_xy.shape[1]
    n_chunks = 6
    chunk_rows = field_rows // n_chunks
    def first_chunk(point_xy, region):
        lid_first, lid_second = lids(region)
        tile = tile_chunk(point_xy[:, :chunk_rows], lid_first[:chunk_rows], lid_second[:chunk_rows])
        return tile, (lid_first, lid_second)

    top_partial = complex_product(stacked_matrix(inv_top), rhs_top)
    works = [((field_xy, region_label), first_chunk)] + [None] * (n_chunks - 1)

    def chunk_work(i, lid_pair):
        rows = slice(i * chunk_rows, (i + 1) * chunk_rows)
        return ((field_xy[:, rows], lid_pair[0][rows], lid_pair[1][rows]), tile_chunk)

    top_solved, tiles_a = col_sum_to_columns(
        top_partial, works=(works[0], None, lambda done: chunk_work(1, done[0][1]))
    )
    lid_pair = tiles_a[0][1]
    tiles_a = [tiles_a[0][0], tiles_a[1]]
    works = [None] + [chunk_work(i, lid_pair) for i in range(1, n_chunks)]
    remainder_cols, tiles_b = col_sum_to_columns(
        complex_product(stacked_matrix(lower_panel), top_solved),
        rhs_bottom,
        works=(works[2], works[3], None),
    )
    bottom_solved, tiles_c = col_sum_to_columns(
        complex_product(stacked_matrix(inv_bottom), remainder_cols),
        works=(works[4], works[5], None),
    )
    tile_chunks = tiles_a + tiles_b + tiles_c
    strengths = jnp.stack([top_solved, bottom_solved])
    weights = strengths.astype(jnp.bfloat16)
    right_count = weights.shape[3]
    src_real = weights[:, 0].reshape(-1, right_count)
    src_imag = weights[:, 1].reshape(-1, right_count)
    for_real = jnp.concatenate([src_real, src_imag], axis=1)
    for_imag = jnp.concatenate([-src_imag, src_real], axis=1)
    result = jnp.concatenate(
        [
            jnp.dot(tile_real, for_real, preferred_element_type=jnp.float32)
            + jnp.dot(tile_imag, for_imag, preferred_element_type=jnp.float32)
            for tile_real, tile_imag in tile_chunks
        ],
        axis=0,
    )
    out_rows = field_rows // n_col
    split = result.reshape(n_col, out_rows, 2 * right_count)
    summed = lax.all_to_all(split, "col", 0, 0, tiled=True).sum(0)
    elevation = summed.reshape(out_rows, 2, right_count)
    return (strengths, elevation)


def solution(mesh):
    n_row = mesh.shape["row"]
    split_mesh = Mesh(
        mesh.devices.reshape(n_row // 2, 2, mesh.shape["col"]), ("z", "core", "col")
    )
    row = ("z", "core")
    in_specs = (
        P(None, row, "col"),
        P(None, row, "col"),
        P(None, row, "col"),
        P(None, "col", None),
        P(None, row, None),
        P(None, None, "col"),
        P(None, "col"),
        P(None, "col"),
        P(None, row),
        P(row),
        P(),
        P(),
    )
    out_specs = (P(None, None, "col", None), P(("z", "core", "col"), None, None))
    return jax.shard_map(
        per_device, mesh=split_mesh, in_specs=in_specs, out_specs=out_specs, check_vma=False
    )
```

```python
import jax
import jax.numpy as jnp
from jax import lax
from jax.sharding import Mesh, PartitionSpec as P


def stacked_matrix(matrix):
    return jnp.concatenate(
        [
            jnp.concatenate([matrix[0], -matrix[1]], axis=1),
            jnp.concatenate([matrix[1], matrix[0]], axis=1),
        ],
        axis=0,
    )


def complex_product(stacked, vector):
    parts, rows, right = vector.shape
    product = jnp.dot(
        stacked,
        vector.reshape(parts * rows, right),
        precision=lax.Precision.HIGHEST,
        preferred_element_type=jnp.float32,
    )
    return product.reshape(parts, stacked.shape[0] // parts, right)


def green_tile(point_x, point_y, lid_first, lid_second, source_x, source_y, depth_sq, depth_term, src_label, wave_value):
    delta_x = point_x[:, None] - source_x[None, :]
    delta_y = point_y[:, None] - source_y[None, :]
    distance = jnp.sqrt(delta_x * delta_x + delta_y * delta_y + depth_sq[None, :])
    factor = jnp.where(src_label[None, :] == 1, lid_second[:, None], lid_first[:, None])
    amplitude = factor * depth_term[None, :] / distance
    phase_angle = wave_value * distance
    return (
        (amplitude * jnp.cos(phase_angle)).astype(jnp.bfloat16),
        (amplitude * jnp.sin(phase_angle)).astype(jnp.bfloat16),
    )


def beside(step, value, work):
    if work is None:
        return step(value), None
    inputs, fn = work
    value, inputs = lax.optimization_barrier((value, inputs))
    result = step(value)
    done = fn(*inputs)
    return lax.optimization_barrier((result, done))


def col_sum_to_columns(partial, offset=None, works=(None, None, None)):
    n_col = lax.axis_size("col")
    n_z = lax.axis_size("z")
    parts, rows, right = partial.shape
    piece = rows // n_col
    outputs = []

    def col_step(value):
        return lax.all_to_all(value, "col", 0, 0, tiled=True)

    def z_step(value):
        return lax.all_to_all(value, "z", 0, 0, tiled=True)

    split = partial.reshape(parts, n_col, piece, right).transpose(1, 0, 2, 3)
    scattered, out = beside(col_step, split, works[0])
    outputs.append(out)
    summed = scattered.sum(0)
    if offset is not None:
        start = lax.axis_index("col") * piece
        summed = lax.dynamic_slice_in_dim(offset, start, piece, 1) - summed
    spread = jnp.broadcast_to(summed[None], (n_z,) + summed.shape)
    middle_work = works[1](outputs) if callable(works[1]) else works[1]
    gathered, out = beside(z_step, spread, middle_work)
    outputs.append(out)
    last_work = works[2](outputs) if callable(works[2]) else works[2]
    moved, out = beside(col_step, gathered, last_work)
    outputs.append(out)
    block = moved.transpose(1, 0, 2, 3).reshape(parts, rows, right)
    other = lax.ppermute(block, "core", [(0, 1), (1, 0)])
    first_core = lax.axis_index("core") == 0
    vector = jnp.concatenate(
        [jnp.where(first_core, block, other), jnp.where(first_core, other, block)], axis=1
    )
    return vector, [o for o in outputs if o is not None]


def per_device(
    inv_top,
    inv_bottom,
    lower_panel,
    rhs_top,
    rhs_bottom,
    source_xy,
    source_depth,
    body_label,
    field_xy,
    region_label,
    lid_table,
    wave_number,
):
    n_col = lax.axis_size("col")
    source_x = source_xy[0].reshape(-1)
    source_y = source_xy[1].reshape(-1)
    src_depth = source_depth.reshape(-1)
    src_label = body_label.reshape(-1)
    wave_value = wave_number[0]

    depth_sq = src_depth * src_depth
    depth_term = jnp.exp(wave_value * src_depth)
    def lids(region):
        return (
            jnp.where(region == 1, lid_table[1, 0], lid_table[0, 0]),
            jnp.where(region == 1, lid_table[1, 1], lid_table[0, 1]),
        )

    def tile_chunk(point_xy, first, second):
        return green_tile(
            point_xy[0],
            point_xy[1],
            first,
            second,
            source_x,
            source_y,
            depth_sq,
            depth_term,
            src_label,
            wave_value,
        )

    field_rows = field_xy.shape[1]
    n_chunks = 6
    chunk_rows = field_rows // n_chunks
    def first_chunk(point_xy, region):
        lid_first, lid_second = lids(region)
        tile = tile_chunk(point_xy[:, :chunk_rows], lid_first[:chunk_rows], lid_second[:chunk_rows])
        return tile, (lid_first, lid_second)

    top_partial = complex_product(stacked_matrix(inv_top), rhs_top)
    works = [((field_xy, region_label), first_chunk)] + [None] * (n_chunks - 1)

    def chunk_work(i, lid_pair):
        rows = slice(i * chunk_rows, (i + 1) * chunk_rows)
        return ((field_xy[:, rows], lid_pair[0][rows], lid_pair[1][rows]), tile_chunk)

    top_solved, tiles_a = col_sum_to_columns(
        top_partial, works=(works[0], lambda done: chunk_work(1, done[0][1]), None)
    )
    lid_pair = tiles_a[0][1]
    tiles_a = [tiles_a[0][0], tiles_a[1]]
    works = [None] + [chunk_work(i, lid_pair) for i in range(1, n_chunks)]
    remainder_cols, tiles_b = col_sum_to_columns(
        complex_product(stacked_matrix(lower_panel), top_solved),
        rhs_bottom,
        works=(works[2], works[3], None),
    )
    bottom_solved, tiles_c = col_sum_to_columns(
        complex_product(stacked_matrix(inv_bottom), remainder_cols),
        works=(works[4], works[5], None),
    )
    tile_chunks = tiles_a + tiles_b + tiles_c
    strengths = jnp.stack([top_solved, bottom_solved])
    weights = strengths.astype(jnp.bfloat16)
    right_count = weights.shape[3]
    src_real = weights[:, 0].reshape(-1, right_count)
    src_imag = weights[:, 1].reshape(-1, right_count)
    for_real = jnp.concatenate([src_real, src_imag], axis=1)
    for_imag = jnp.concatenate([-src_imag, src_real], axis=1)
    result = jnp.concatenate(
        [
            jnp.dot(tile_real, for_real, preferred_element_type=jnp.float32)
            + jnp.dot(tile_imag, for_imag, preferred_element_type=jnp.float32)
            for tile_real, tile_imag in tile_chunks
        ],
        axis=0,
    )
    out_rows = field_rows // n_col
    split = result.reshape(n_col, out_rows, 2 * right_count)
    summed = lax.all_to_all(split, "col", 0, 0, tiled=True).sum(0)
    elevation = summed.reshape(out_rows, 2, right_count)
    return (strengths, elevation)


def solution(mesh):
    n_row = mesh.shape["row"]
    split_mesh = Mesh(
        mesh.devices.reshape(n_row // 2, 2, mesh.shape["col"]), ("z", "core", "col")
    )
    row = ("z", "core")
    in_specs = (
        P(None, row, "col"),
        P(None, row, "col"),
        P(None, row, "col"),
        P(None, "col", None),
        P(None, row, None),
        P(None, None, "col"),
        P(None, "col"),
        P(None, "col"),
        P(None, row),
        P(row),
        P(),
        P(),
    )
    out_specs = (P(None, None, "col", None), P(("z", "core", "col"), None, None))
    return jax.shard_map(
        per_device, mesh=split_mesh, in_specs=in_specs, out_specs=out_specs, check_vma=False
    )
```
